512 devices in a mesh: fsdp: 16 (over y, core), expert: 32 (over x, z).
Axes of the slice: x: 4, y: 8, z: 8, core: 2. Of those that a mesh axis runs over, the one named last changes fastest.
Arguments:
- frames: bfloat16 [16, 4096, 1536], P('fsdp', 'expert'), may hold values from -6 to 6
- ln_gain: float32 [1536], replicated, may hold values from 0.5 to 1.5
- kernel: float32 [31, 1536], replicated, may hold values from -1 to 1
- bn_scale: float32 [1536], replicated, may hold values from 0.5 to 2
- bn_shift: float32 [1536], replicated, may hold values from -1 to 1
- ffn_gain: float32 [1536], replicated, may hold values from 0.5 to 1.5
- expert_ids: int32 [16, 4096, 2], P('fsdp', 'expert'), may hold values from 0 to 31, all different within a row; in each aligned block of 128 rows (0 to 127, 128 to 255, ..., all dimensions but the last counted through in order) at most 16 rows name the same one
- gates: float32 [16, 4096, 2], P('fsdp', 'expert'), may hold values from 0.1 to 1
- w_in: bfloat16 [32, 1536, 1536], P('expert', 'fsdp'), may hold values from -0.15625 to 0.15625
- w_out: bfloat16 [32, 1536, 1536], P('expert', 'fsdp'), may hold values from -0.15625 to 0.15625
Outputs:
- layer_out: bfloat16 [16, 4096, 1536], P('fsdp', 'expert')
The draws below stay inside these ranges and needn't reach their ends.
Inputs may be any that keep to these rules, and one draw needn't show every extreme that they name: `expert_ids`: the 2 experts of a frame differ; within the 128 frames of one device (aligned blocks along a sequence) no expert is named more than 16 times, a bound that some block reaches.
All inputs are finite; a program needn't handle non-finite values.
Results may differ from the reference program's by a relative error of at most 0.0039.
Values may be sent and summed in bfloat16 or wider, within the bound.
No kernel may reach another device: no remote copies, remote signals or barrier semaphores. Data moves between devices by JAX's collectives and lax.ppermute only.
A program may use at most 64 MiB of HBM per device.

```python
import math
import jax
import jax.numpy as jnp
import numpy as np
from jax import lax

D = 1536
HID = 1536
KERNEL = 31
TOP = 2
TOK_DEV = 128
EXPERTS = 32
CAP = 16
SEQS = 16
LENGTH = 4096
N_EXPERT = 32


def levels(stream_key, dims, split, least, top_value):
    level = 1.0
    for axis_at, parts in split:
        steps = jax.random.uniform(jax.random.fold_in(jax.random.fold_in(stream_key, 6), axis_at), (parts,), jnp.float32, least / len(split), top_value / len(split))
        level = level * jnp.repeat(jnp.exp(steps), dims[axis_at] // parts).reshape((-1,) + (1,) * (len(dims) - 1 - axis_at))
    return level


def deal_out(key, own, number, rows, number_of, top, most, slope):
    ranking = jax.random.permutation(key, number_of)
    packed, usual = load_shares(number_of, rows * top, most, slope, True), load_shares(number_of, rows * top, most, slope, False)
    places = jnp.arange(number_of)

    def named(sizes, turn):
        used = int((sizes > 0).sum())
        fixed = max(1, used // 4)
        passed = fixed + (places - fixed + turn * (used - fixed)) % max(1, number_of - fixed)
        return jnp.zeros((number_of,), jnp.int32).at[ranking[jnp.where(places < fixed, places, passed)]].set(jnp.asarray(sizes, jnp.int32))

    sizes = jnp.where(number % 4 == 0, named(packed, number // 4), named(usual, number - number // 4 - 1))
    mixed = jax.random.permutation(jax.random.fold_in(own, 3), number_of)
    source_of, taker = mixed[0:number_of // 2 * 2:2], mixed[1:number_of // 2 * 2:2]
    margin = jnp.minimum(sizes[source_of] - 1, most - sizes[taker]) // 2
    margin = jnp.where((source_of == ranking[0]) | (taker == ranking[0]) | (sizes[taker] == 0), 0, jnp.maximum(margin, 0))
    passed = jax.random.randint(jax.random.fold_in(own, 4), (number_of // 2,), 0, 1 << 20) % (margin + 1)
    sizes = sizes.at[source_of].add(-passed).at[taker].add(passed)
    items = jnp.searchsorted(jnp.cumsum(sizes), jnp.arange(rows * top), side="right").astype(jnp.int32)
    listing = items.reshape(top, rows).T
    listing = listing[jax.random.permutation(jax.random.fold_in(own, 1), rows)]
    turn = jax.random.randint(jax.random.fold_in(own, 2), (rows, 1), 0, top)
    return jnp.take_along_axis(listing, (jnp.arange(top)[None, :] + turn) % top, axis=1)


def load_shares(number_of, total, bound, lean, full):
    loads = [(1 << 20) // math.isqrt(rank ** lean) + 1 for rank in range(1, number_of + 1)]
    largest = bound if full else min(bound, max(-(-total // number_of), total * loads[0] // sum(loads)))
    least = 1 if total - largest >= number_of - 1 else 0
    given, rest = [largest] + [least] * (number_of - 1), total - largest - least * (number_of - 1)
    while rest > 0:
        movable = [i for i in range(1, number_of) if given[i] < largest] or [i for i in range(1, number_of) if given[i] < bound]
        whole, remaining = sum([loads[i] for i in movable]), rest
        for i in movable:
            extra = min(bound - given[i], max(1, remaining * loads[i] // whole), rest)
            given[i] = given[i] + extra
            rest = rest - extra
    return np.array(given)


def bell_draw(key, shape, width, bound, cuts=(), held_as=jnp.bfloat16):
    loudness = levels(key, shape, cuts, -0.22, 0.18) if cuts else 1.0
    array = jax.random.normal(key, shape, jnp.float32) * width * loudness
    return jnp.minimum(jnp.maximum(array, -bound), bound).astype(held_as)


def setup_inputs(seed: int = 0) -> dict:
    arg_keys = jax.random.split(jax.random.key(seed), 11)
    frames = bell_draw(arg_keys[0], (SEQS, LENGTH, D), 1.0, 6.0, ((0, 16), (1, 32)))
    ln_gain = jnp.clip(1.0 + 0.1 * jax.random.normal(arg_keys[1], (D,), jnp.float32), 0.5, 1.5)
    kernel = bell_draw(arg_keys[2], (KERNEL, D), KERNEL ** -0.5, 1.0, (), jnp.float32)
    bn_scale = jnp.clip(jnp.exp(jax.random.uniform(arg_keys[3], (D,), jnp.float32, math.log(0.5), math.log(2.0))), 0.5, 2.0)
    bn_shift = jnp.clip(jax.random.uniform(arg_keys[4], (D,), jnp.float32, -1.0, 1.0), -1.0, 1.0)
    ffn_gain = jnp.clip(1.0 + 0.1 * jax.random.normal(arg_keys[5], (D,), jnp.float32), 0.5, 1.5)
    expert_ids_keys = jax.random.split(jax.random.fold_in(arg_keys[6], 1), SEQS * LENGTH // TOK_DEV)
    expert_ids_turns = jax.random.permutation(jax.random.fold_in(arg_keys[6], 3), SEQS * LENGTH // TOK_DEV)
    expert_ids = jax.vmap(lambda own, number: deal_out(jax.random.fold_in(arg_keys[6], 2), own, number, TOK_DEV, EXPERTS, TOP, CAP, 2))(expert_ids_keys, expert_ids_turns).reshape((SEQS, LENGTH, TOP))
    gates = jnp.clip(0.1 + 0.9 * jax.random.uniform(arg_keys[7], (SEQS, LENGTH, TOP), jnp.float32) ** levels(arg_keys[7], (SEQS, LENGTH, TOP), ((0, 16), (1, 32)), -0.2, 0.2), 0.1, 1.0)
    w_in = bell_draw(arg_keys[8], (EXPERTS, D, HID), D ** -0.5, 0.15625, ((0, 32), (1, 16)))
    w_out = bell_draw(arg_keys[9], (EXPERTS, HID, D), HID ** -0.5, 0.15625, ((0, 32), (1, 16)))
    return {"frames": frames, "ln_gain": ln_gain, "kernel": kernel, "bn_scale": bn_scale, "bn_shift": bn_shift, "ffn_gain": ffn_gain, "expert_ids": expert_ids, "gates": gates, "w_in": w_in, "w_out": w_out}


eps_norm = 1e-05

def layer_norm(values, gain):
    centre = lax.optimization_barrier(jnp.mean(values, axis=-1, keepdims=True))
    centred = values - centre
    spread = lax.optimization_barrier(jnp.mean(centred * centred, axis=-1, keepdims=True))
    return centred * lax.rsqrt(spread + eps_norm) * gain

def expert_ffn(operands):
    rows_in, first, second = operands
    hidden = jax.nn.silu(jnp.dot(rows_in, first, preferred_element_type=jnp.float32)).astype(jnp.bfloat16)
    return jnp.dot(hidden, second, preferred_element_type=jnp.float32).astype(jnp.bfloat16)

def reference(frames, ln_gain, kernel, bn_scale, bn_shift, ffn_gain, expert_ids, gates, w_in, w_out):
    reach = (KERNEL - 1) // 2
    stream = frames.astype(jnp.float32)
    normed = layer_norm(stream, ln_gain).astype(jnp.bfloat16)
    padded = jnp.pad(normed.astype(jnp.float32), ((0, 0), (reach, reach), (0, 0)))
    filtered = jnp.zeros(stream.shape, jnp.float32)
    for offset in range(KERNEL):
        filtered = filtered + kernel[offset] * padded[:, offset:offset + LENGTH]
    mixed = stream + jax.nn.silu(bn_scale * filtered + bn_shift)
    routed = layer_norm(mixed, ffn_gain).astype(jnp.bfloat16)
    blocks = SEQS * N_EXPERT
    chosen = expert_ids.reshape(blocks, TOK_DEV * TOP).astype(jnp.int32)
    onehot = (chosen[:, :, None] == jnp.arange(EXPERTS, dtype=jnp.int32)[None, None, :]).astype(jnp.int32)
    before = jnp.cumsum(onehot, axis=1) - onehot
    slot_at = lax.optimization_barrier(jnp.sum(before * onehot, axis=2))
    row_at = (jnp.arange(blocks, dtype=jnp.int32)[:, None] * CAP + slot_at).astype(jnp.int32)
    source = jnp.repeat(routed.reshape(blocks, TOK_DEV, D), TOP, axis=1)
    buffers = jnp.zeros((EXPERTS, blocks * CAP, D), jnp.bfloat16).at[chosen, row_at].set(source)
    results = lax.map(expert_ffn, (buffers, w_in, w_out))
    picked = results[chosen, row_at].reshape(SEQS, LENGTH, TOP, D).astype(jnp.float32)
    combined = lax.optimization_barrier(jnp.sum(gates[..., None] * picked, axis=2))
    return (mixed + 0.5 * combined).astype(jnp.bfloat16)
```

```python
import jax
import jax.numpy as jnp
from jax import lax
from jax.sharding import PartitionSpec as P

eps_norm = 1e-05


def padded_2(block, sides, width):
    for axis, dim in sides:
        count = lax.axis_size(axis)
        forward = [(i, i + 1) for i in range(count - 1)]
        backward = [(target, source) for source, target in forward]
        low = lax.ppermute(
            lax.slice_in_dim(block, block.shape[dim] - width, None, axis=dim), axis, forward
        )
        high = lax.ppermute(lax.slice_in_dim(block, 0, width, axis=dim), axis, backward)
        block = jnp.concatenate([low, block, high], axis=dim)
    return block


def layer_norm(values, gain):
    centre = jnp.mean(values, axis=-1, keepdims=True)
    centred = values - centre
    spread = jnp.mean(centred * centred, axis=-1, keepdims=True)
    return centred * lax.rsqrt(spread + eps_norm) * gain


def shards(frames, ln_gain, kernel, bn_scale, bn_shift, ffn_gain, expert_ids, gates, w_in, w_out):
    frame_count = frames.shape[1]
    width = frames.shape[2]
    taps = kernel.shape[0]
    reach = (taps - 1) // 2
    picks_per = expert_ids.shape[2]
    experts_all = lax.axis_size("expert") * w_in.shape[0]
    capacity = 2 * picks_per * frame_count // experts_all
    slots_all = experts_all * capacity
    stream = frames[0].astype(jnp.float32)
    normed = layer_norm(stream, ln_gain).astype(jnp.bfloat16)
    padded = padded_2(normed, (("expert", 0),), reach)
    filtered = jnp.zeros(stream.shape, jnp.float32)
    for offset in range(taps):
        filtered = filtered + kernel[offset] * padded[offset : offset + frame_count]
    mixed = stream + jax.nn.silu(bn_scale * filtered + bn_shift)
    routed = layer_norm(mixed, ffn_gain).astype(jnp.bfloat16)
    chosen = expert_ids[0].reshape(-1)
    onehot = (chosen[:, None] == jnp.arange(experts_all, dtype=jnp.int32)[None, :]).astype(
        jnp.int32
    )
    before = jnp.cumsum(onehot, axis=0) - onehot
    slot_at = jnp.sum(before * onehot, axis=1)
    target = (chosen * capacity + slot_at).reshape(frame_count, picks_per)
    placing = jnp.any(
        target[None, :, :] == jnp.arange(slots_all, dtype=jnp.int32)[:, None, None], axis=2
    )
    outgoing = jnp.dot(placing.astype(jnp.bfloat16), routed, preferred_element_type=jnp.float32)
    outgoing = outgoing.astype(jnp.bfloat16).reshape(experts_all, capacity, width)
    chunks = 2
    piece = width // chunks
    full_in = lax.all_gather(w_in, "fsdp", axis=1, tiled=True)
    out_pieces = [
        lax.all_gather(w_out[:, :, j * piece : (j + 1) * piece], "fsdp", axis=1, tiled=True)
        for j in range(chunks)
    ]
    block = lax.all_to_all(outgoing, "expert", split_axis=0, concat_axis=0, tiled=True)
    rows_in = block.reshape(-1, width)
    hidden = jax.nn.silu(jnp.dot(rows_in, full_in[0], preferred_element_type=jnp.float32)).astype(
        jnp.bfloat16
    )
    parts = []
    for j in range(chunks):
        result = jnp.dot(hidden, out_pieces[j][0], preferred_element_type=jnp.float32).astype(
            jnp.bfloat16
        )
        returned = lax.all_to_all(
            result.reshape(experts_all, capacity, piece), "expert", split_axis=0, concat_axis=0, tiled=True
        )
        rows_back = returned.reshape(-1, piece)
        picked = (
            jnp.take(rows_back, target.reshape(-1), axis=0)
            .reshape(frame_count, picks_per, piece)
            .astype(jnp.float32)
        )
        parts.append(jnp.sum(gates[0][:, :, None] * picked, axis=1))
    combined = jnp.concatenate(parts, axis=1)
    return (mixed + 0.5 * combined).astype(jnp.bfloat16)[None]


def solution(mesh):
    return jax.shard_map(
        shards,
        mesh=mesh,
        in_specs=(
            P("fsdp", "expert", None),
            P(),
            P(),
            P(),
            P(),
            P(),
            P("fsdp", "expert", None),
            P("fsdp", "expert", None),
            P("expert", "fsdp", None),
            P("expert", "fsdp", None),
        ),
        out_specs=P("fsdp", "expert", None),
        check_vma=False,
    )
```

```python
import jax
import jax.numpy as jnp
from jax import lax
from jax.sharding import PartitionSpec as P

eps_norm = 1e-05


def padded_2(block, sides, width):
    for axis, dim in sides:
        count = lax.axis_size(axis)
        forward = [(i, i + 1) for i in range(count - 1)]
        backward = [(target, source) for source, target in forward]
        low = lax.ppermute(
            lax.slice_in_dim(block, block.shape[dim] - width, None, axis=dim), axis, forward
        )
        high = lax.ppermute(lax.slice_in_dim(block, 0, width, axis=dim), axis, backward)
        block = jnp.concatenate([low, block, high], axis=dim)
    return block


def layer_norm(values, gain):
    centre = jnp.mean(values, axis=-1, keepdims=True)
    centred = values - centre
    spread = jnp.mean(centred * centred, axis=-1, keepdims=True)
    return centred * lax.rsqrt(spread + eps_norm) * gain


def shards(frames, ln_gain, kernel, bn_scale, bn_shift, ffn_gain, expert_ids, gates, w_in, w_out):
    frame_count = frames.shape[1]
    width = frames.shape[2]
    taps = kernel.shape[0]
    reach = (taps - 1) // 2
    picks_per = expert_ids.shape[2]
    experts_all = lax.axis_size("expert") * w_in.shape[0]
    capacity = 2 * picks_per * frame_count // experts_all
    slots_all = experts_all * capacity
    stream = frames[0].astype(jnp.float32)
    normed = layer_norm(stream, ln_gain).astype(jnp.bfloat16)
    padded = padded_2(normed, (("expert", 0),), reach)
    filtered = jnp.zeros(stream.shape, jnp.float32)
    for offset in range(taps):
        filtered = filtered + kernel[offset] * padded[offset : offset + frame_count]
    mixed = stream + jax.nn.silu(bn_scale * filtered + bn_shift)
    routed = layer_norm(mixed, ffn_gain).astype(jnp.bfloat16)
    chosen = expert_ids[0].reshape(-1)
    onehot = (chosen[:, None] == jnp.arange(experts_all, dtype=jnp.int32)[None, :]).astype(
        jnp.int32
    )
    before = jnp.cumsum(onehot, axis=0) - onehot
    slot_at = jnp.sum(before * onehot, axis=1)
    target = (chosen * capacity + slot_at).reshape(frame_count, picks_per)
    placing = jnp.any(
        target[None, :, :] == jnp.arange(slots_all, dtype=jnp.int32)[:, None, None], axis=2
    )
    outgoing = jnp.dot(placing.astype(jnp.bfloat16), routed, preferred_element_type=jnp.float32)
    outgoing = outgoing.astype(jnp.bfloat16).reshape(experts_all, capacity, width)
    both = lax.all_gather(jnp.concatenate([w_in, w_out], axis=0), "fsdp", axis=1, tiled=True)
    full_in, full_out = both[0:1], both[1:2]
    block = lax.all_to_all(outgoing, "expert", split_axis=0, concat_axis=0, tiled=True)
    rows_in = block.reshape(-1, width)
    hidden = jax.nn.silu(jnp.dot(rows_in, full_in[0], preferred_element_type=jnp.float32)).astype(
        jnp.bfloat16
    )
    result = jnp.dot(hidden, full_out[0], preferred_element_type=jnp.float32).astype(jnp.bfloat16)
    returned = lax.all_to_all(
        result.reshape(block.shape), "expert", split_axis=0, concat_axis=0, tiled=True
    )
    rows_back = returned.reshape(-1, width)
    picked = (
        jnp.take(rows_back, target.reshape(-1), axis=0)
        .reshape(frame_count, picks_per, width)
        .astype(jnp.float32)
    )
    combined = jnp.sum(gates[0][:, :, None] * picked, axis=1)
    return (mixed + 0.5 * combined).astype(jnp.bfloat16)[None]


def solution(mesh):
    return jax.shard_map(
        shards,
        mesh=mesh,
        in_specs=(
            P("fsdp", "expert", None),
            P(),
            P(),
            P(),
            P(),
            P(),
            P("fsdp", "expert", None),
            P("fsdp", "expert", None),
            P("expert", "fsdp", None),
            P("expert", "fsdp", None),
        ),
        out_specs=P("fsdp", "expert", None),
        check_vma=False,
    )
```

```python
import jax
import jax.numpy as jnp
from jax import lax
from jax.sharding import PartitionSpec as P

eps_norm = 1e-05


def padded_2(block, sides, width):
    for axis, dim in sides:
        count = lax.axis_size(axis)
        forward = [(i, i + 1) for i in range(count - 1)]
        backward = [(target, source) for source, target in forward]
        low = lax.ppermute(
            lax.slice_in_dim(block, block.shape[dim] - width, None, axis=dim), axis, forward
        )
        high = lax.ppermute(lax.slice_in_dim(block, 0, width, axis=dim), axis, backward)
        block = jnp.concatenate([low, block, high], axis=dim)
    return block


def layer_norm(values, gain):
    centre = jnp.mean(values, axis=-1, keepdims=True)
    centred = values - centre
    spread = jnp.mean(centred * centred, axis=-1, keepdims=True)
    return centred * lax.rsqrt(spread + eps_norm) * gain


def shards(frames, ln_gain, kernel, bn_scale, bn_shift, ffn_gain, expert_ids, gates, w_in, w_out):
    frame_count = frames.shape[1]
    width = frames.shape[2]
    taps = kernel.shape[0]
    reach = (taps - 1) // 2
    picks_per = expert_ids.shape[2]
    experts_all = lax.axis_size("expert") * w_in.shape[0]
    capacity = 2 * picks_per * frame_count // experts_all
    slots_all = experts_all * capacity
    both = lax.all_gather(jnp.concatenate([w_in, w_out], axis=0), "fsdp", axis=1, tiled=True)
    full_in, full_out = both[0:1], both[1:2]
    raw = padded_2(frames[0], (("expert", 0),), reach)
    padded = layer_norm(raw.astype(jnp.float32), ln_gain).astype(jnp.bfloat16)
    stream = frames[0].astype(jnp.float32)
    filtered = jnp.zeros(stream.shape, jnp.float32)
    for offset in range(taps):
        filtered = filtered + kernel[offset] * padded[offset : offset + frame_count]
    mixed = stream + jax.nn.silu(bn_scale * filtered + bn_shift)
    routed = layer_norm(mixed, ffn_gain).astype(jnp.bfloat16)
    chosen = expert_ids[0].reshape(-1)
    picks = chosen.shape[0]
    onehot = (chosen[:, None] == jnp.arange(experts_all, dtype=jnp.int32)[None, :]).astype(
        jnp.bfloat16
    )
    lower = (
        jnp.arange(picks, dtype=jnp.int32)[:, None] > jnp.arange(picks, dtype=jnp.int32)[None, :]
    ).astype(jnp.bfloat16)
    before = jnp.dot(lower, onehot, preferred_element_type=jnp.float32)
    slot_at = jnp.sum(before * onehot.astype(jnp.float32), axis=1).astype(jnp.int32)
    target = (chosen * capacity + slot_at).reshape(frame_count, picks_per)
    placing = jnp.any(
        target[None, :, :] == jnp.arange(slots_all, dtype=jnp.int32)[:, None, None], axis=2
    )
    outgoing = jnp.dot(placing.astype(jnp.bfloat16), routed, preferred_element_type=jnp.float32)
    outgoing = outgoing.astype(jnp.bfloat16).reshape(experts_all, capacity, width)
    block = lax.all_to_all(outgoing, "expert", split_axis=0, concat_axis=0, tiled=True)
    rows_in = block.reshape(-1, width)
    hidden = jax.nn.silu(jnp.dot(rows_in, full_in[0], preferred_element_type=jnp.float32)).astype(
        jnp.bfloat16
    )
    result = jnp.dot(hidden, full_out[0], preferred_element_type=jnp.float32).astype(jnp.bfloat16)
    returned = lax.all_to_all(
        result.reshape(block.shape), "expert", split_axis=0, concat_axis=0, tiled=True
    )
    rows_back = returned.reshape(-1, width)
    select = (
        target.reshape(-1)[:, None] == jnp.arange(slots_all, dtype=jnp.int32)[None, :]
    ).astype(jnp.bfloat16)
    picked = jnp.dot(select, rows_back, preferred_element_type=jnp.float32).reshape(
        frame_count, picks_per, width
    )
    combined = gates[0][:, 0][:, None] * picked[:, 0]
    for k in range(1, picks_per):
        combined = combined + gates[0][:, k][:, None] * picked[:, k]
    return (mixed + 0.5 * combined).astype(jnp.bfloat16)[None]


def solution(mesh):
    return jax.shard_map(
        shards,
        mesh=mesh,
        in_specs=(
            P("fsdp", "expert", None),
            P(),
            P(),
            P(),
            P(),
            P(),
            P("fsdp", "expert", None),
            P("fsdp", "expert", None),
            P("expert", "fsdp", None),
            P("expert", "fsdp", None),
        ),
        out_specs=P("fsdp", "expert", None),
        check_vma=False,
    )
```

```python
import jax
import jax.numpy as jnp
from jax import lax
from jax.experimental import pallas as pl
from jax.experimental.pallas import tpu as pltpu
from jax.sharding import PartitionSpec as P

eps_norm = 1e-05


def padded_2(block, sides, width):
    for axis, dim in sides:
        count = lax.axis_size(axis)
        forward = [(i, i + 1) for i in range(count - 1)]
        backward = [(target, source) for source, target in forward]
        low = lax.ppermute(
            lax.slice_in_dim(block, block.shape[dim] - width, None, axis=dim), axis, forward
        )
        high = lax.ppermute(lax.slice_in_dim(block, 0, width, axis=dim), axis, backward)
        block = jnp.concatenate([low, block, high], axis=dim)
    return block


def stack_pair(first, second):
    def body(first_ref, second_ref, out_ref, sems):
        copies = (
            pltpu.make_async_copy(first_ref, out_ref.at[0:1], sems.at[0]),
            pltpu.make_async_copy(second_ref, out_ref.at[1:2], sems.at[1]),
        )
        for copy in copies:
            copy.start()
        for copy in copies:
            copy.wait()

    return pl.pallas_call(
        body,
        out_shape=jax.ShapeDtypeStruct((2,) + first.shape[1:], first.dtype),
        in_specs=[pl.BlockSpec(memory_space=pl.ANY), pl.BlockSpec(memory_space=pl.ANY)],
        out_specs=pl.BlockSpec(memory_space=pl.ANY),
        scratch_shapes=[pltpu.SemaphoreType.DMA((2,))],
    )(first, second)


def layer_norm(values, gain):
    centre = jnp.mean(values, axis=-1, keepdims=True)
    centred = values - centre
    spread = jnp.mean(centred * centred, axis=-1, keepdims=True)
    return centred * lax.rsqrt(spread + eps_norm) * gain


def shards(frames, ln_gain, kernel, bn_scale, bn_shift, ffn_gain, expert_ids, gates, w_in, w_out):
    frame_count = frames.shape[1]
    width = frames.shape[2]
    taps = kernel.shape[0]
    reach = (taps - 1) // 2
    picks_per = expert_ids.shape[2]
    experts_all = lax.axis_size("expert") * w_in.shape[0]
    capacity = 2 * picks_per * frame_count // experts_all
    slots_all = experts_all * capacity
    both = lax.all_gather(stack_pair(w_in, w_out), "fsdp", axis=1, tiled=True)
    full_in, full_out = both[0:1], both[1:2]
    raw = padded_2(frames[0], (("expert", 0),), reach)
    padded = layer_norm(raw.astype(jnp.float32), ln_gain).astype(jnp.bfloat16)
    stream = frames[0].astype(jnp.float32)
    filtered = jnp.zeros(stream.shape, jnp.float32)
    for offset in range(taps):
        filtered = filtered + kernel[offset] * padded[offset : offset + frame_count]
    mixed = stream + jax.nn.silu(bn_scale * filtered + bn_shift)
    routed = layer_norm(mixed, ffn_gain).astype(jnp.bfloat16)
    chosen = expert_ids[0].reshape(-1)
    picks = chosen.shape[0]
    onehot = (chosen[:, None] == jnp.arange(experts_all, dtype=jnp.int32)[None, :]).astype(
        jnp.bfloat16
    )
    lower = (
        jnp.arange(picks, dtype=jnp.int32)[:, None] > jnp.arange(picks, dtype=jnp.int32)[None, :]
    ).astype(jnp.bfloat16)
    before = jnp.dot(lower, onehot, preferred_element_type=jnp.float32)
    slot_at = jnp.sum(before * onehot.astype(jnp.float32), axis=1).astype(jnp.int32)
    target = (chosen * capacity + slot_at).reshape(frame_count, picks_per)
    placing = jnp.any(
        target[None, :, :] == jnp.arange(slots_all, dtype=jnp.int32)[:, None, None], axis=2
    )
    outgoing = jnp.dot(placing.astype(jnp.bfloat16), routed, preferred_element_type=jnp.float32)
    outgoing = outgoing.astype(jnp.bfloat16).reshape(experts_all, capacity, width)
    block = lax.all_to_all(outgoing, "expert", split_axis=0, concat_axis=0, tiled=True)
    rows_in = block.reshape(-1, width)
    hidden = jax.nn.silu(jnp.dot(rows_in, full_in[0], preferred_element_type=jnp.float32)).astype(
        jnp.bfloat16
    )
    result = jnp.dot(hidden, full_out[0], preferred_element_type=jnp.float32).astype(jnp.bfloat16)
    returned = lax.all_to_all(
        result.reshape(block.shape), "expert", split_axis=0, concat_axis=0, tiled=True
    )
    rows_back = returned.reshape(-1, width)
    select = (
        target.reshape(-1)[:, None] == jnp.arange(slots_all, dtype=jnp.int32)[None, :]
    ).astype(jnp.bfloat16)
    picked = jnp.dot(select, rows_back, preferred_element_type=jnp.float32).reshape(
        frame_count, picks_per, width
    )
    combined = gates[0][:, 0][:, None] * picked[:, 0]
    for k in range(1, picks_per):
        combined = combined + gates[0][:, k][:, None] * picked[:, k]
    return (mixed + 0.5 * combined).astype(jnp.bfloat16)[None]


def solution(mesh):
    return jax.shard_map(
        shards,
        mesh=mesh,
        in_specs=(
            P("fsdp", "expert", None),
            P(),
            P(),
            P(),
            P(),
            P(),
            P("fsdp", "expert", None),
            P("fsdp", "expert", None),
            P("expert", "fsdp", None),
            P("expert", "fsdp", None),
        ),
        out_specs=P("fsdp", "expert", None),
        check_vma=False,
    )
```

```python
import jax
import jax.numpy as jnp
from jax import lax
from jax.experimental import pallas as pl
from jax.experimental.pallas import tpu as pltpu
from jax.sharding import PartitionSpec as P

eps_norm = 1e-05


def padded_2(block, sides, width):
    for axis, dim in sides:
        count = lax.axis_size(axis)
        forward = [(i, i + 1) for i in range(count - 1)]
        backward = [(target, source) for source, target in forward]
        low = lax.ppermute(
            lax.slice_in_dim(block, block.shape[dim] - width, None, axis=dim), axis, forward
        )
        high = lax.ppermute(lax.slice_in_dim(block, 0, width, axis=dim), axis, backward)
        block = jnp.concatenate([low, block, high], axis=dim)
    return block


def expert_ffn(rows, both, step=256):
    count, width = rows.shape
    hidden_units = both.shape[2]
    steps = hidden_units // step

    def body(x_ref, first_ref, second_ref, out_ref, acc_ref):
        j = pl.program_id(0)

        @pl.when(j == 0)
        def _():
            acc_ref[...] = jnp.zeros_like(acc_ref)

        h = jnp.dot(x_ref[...], first_ref[...], preferred_element_type=jnp.float32)
        h = (h / (1.0 + jnp.exp(-h))).astype(jnp.bfloat16)
        acc_ref[...] += jnp.dot(h, second_ref[...], preferred_element_type=jnp.float32)

        @pl.when(j == steps - 1)
        def _():
            out_ref[...] = acc_ref[...].astype(out_ref.dtype)

    return pl.pallas_call(
        body,
        grid=(steps,),
        in_specs=[
            pl.BlockSpec((count, width), lambda j: (0, 0)),
            pl.BlockSpec((None, width, step), lambda j: (0, 0, j)),
            pl.BlockSpec((None, step, width), lambda j: (1, j, 0)),
        ],
        out_specs=pl.BlockSpec((count, width), lambda j: (0, 0)),
        out_shape=jax.ShapeDtypeStruct((count, width), jnp.bfloat16),
        scratch_shapes=[pltpu.VMEM((count, width), jnp.float32)],
        compiler_params=pltpu.CompilerParams(dimension_semantics=("arbitrary",)),
        cost_estimate=pl.CostEstimate(
            flops=4 * count * width * hidden_units,
            transcendentals=count * hidden_units,
            bytes_accessed=2 * (2 * count * width + 2 * width * hidden_units),
        ),
    )(rows, both, both)


def layer_norm(values, gain):
    centre = jnp.mean(values, axis=-1, keepdims=True)
    centred = values - centre
    spread = jnp.mean(centred * centred, axis=-1, keepdims=True)
    return centred * lax.rsqrt(spread + eps_norm) * gain


def shards(frames, ln_gain, kernel, bn_scale, bn_shift, ffn_gain, expert_ids, gates, w_in, w_out):
    frame_count = frames.shape[1]
    width = frames.shape[2]
    taps = kernel.shape[0]
    reach = (taps - 1) // 2
    picks_per = expert_ids.shape[2]
    experts_all = lax.axis_size("expert") * w_in.shape[0]
    capacity = 2 * picks_per * frame_count // experts_all
    slots_all = experts_all * capacity
    both = lax.all_gather(jnp.concatenate([w_in, w_out], axis=0), "fsdp", axis=1, tiled=True)
    raw = padded_2(frames[0], (("expert", 0),), reach)
    padded = layer_norm(raw.astype(jnp.float32), ln_gain).astype(jnp.bfloat16)
    stream = frames[0].astype(jnp.float32)
    filtered = jnp.zeros(stream.shape, jnp.float32)
    for offset in range(taps):
        filtered = filtered + kernel[offset] * padded[offset : offset + frame_count]
    mixed = stream + jax.nn.silu(bn_scale * filtered + bn_shift)
    routed = layer_norm(mixed, ffn_gain).astype(jnp.bfloat16)
    chosen = expert_ids[0].reshape(-1)
    picks = chosen.shape[0]
    onehot = (chosen[:, None] == jnp.arange(experts_all, dtype=jnp.int32)[None, :]).astype(
        jnp.bfloat16
    )
    lower = (
        jnp.arange(picks, dtype=jnp.int32)[:, None] > jnp.arange(picks, dtype=jnp.int32)[None, :]
    ).astype(jnp.bfloat16)
    before = jnp.dot(lower, onehot, preferred_element_type=jnp.float32)
    slot_at = jnp.sum(before * onehot.astype(jnp.float32), axis=1).astype(jnp.int32)
    target = (chosen * capacity + slot_at).reshape(frame_count, picks_per)
    placing = jnp.any(
        target[None, :, :] == jnp.arange(slots_all, dtype=jnp.int32)[:, None, None], axis=2
    )
    outgoing = jnp.dot(placing.astype(jnp.bfloat16), routed, preferred_element_type=jnp.float32)
    outgoing = outgoing.astype(jnp.bfloat16).reshape(experts_all, capacity, width)
    block = lax.all_to_all(outgoing, "expert", split_axis=0, concat_axis=0, tiled=True)
    rows_in = block.reshape(-1, width)
    result = expert_ffn(rows_in, both)
    returned = lax.all_to_all(
        result.reshape(block.shape), "expert", split_axis=0, concat_axis=0, tiled=True
    )
    rows_back = returned.reshape(-1, width)
    select = (
        target.reshape(-1)[:, None] == jnp.arange(slots_all, dtype=jnp.int32)[None, :]
    ).astype(jnp.bfloat16)
    picked = jnp.dot(select, rows_back, preferred_element_type=jnp.float32).reshape(
        frame_count, picks_per, width
    )
    combined = gates[0][:, 0][:, None] * picked[:, 0]
    for k in range(1, picks_per):
        combined = combined + gates[0][:, k][:, None] * picked[:, k]
    return (mixed + 0.5 * combined).astype(jnp.bfloat16)[None]


def solution(mesh):
    return jax.shard_map(
        shards,
        mesh=mesh,
        in_specs=(
            P("fsdp", "expert", None),
            P(),
            P(),
            P(),
            P(),
            P(),
            P("fsdp", "expert", None),
            P("fsdp", "expert", None),
            P("expert", "fsdp", None),
            P("expert", "fsdp", None),
        ),
        out_specs=P("fsdp", "expert", None),
        check_vma=False,
    )
```

```python
import jax
import jax.numpy as jnp
from jax import lax
from jax.experimental import pallas as pl
from jax.experimental.pallas import tpu as pltpu
from jax.sharding import PartitionSpec as P

eps_norm = 1e-05


def padded_2(block, sides, width):
    for axis, dim in sides:
        count = lax.axis_size(axis)
        forward = [(i, i + 1) for i in range(count - 1)]
        backward = [(target, source) for source, target in forward]
        low = lax.ppermute(
            lax.slice_in_dim(block, block.shape[dim] - width, None, axis=dim), axis, forward
        )
        high = lax.ppermute(lax.slice_in_dim(block, 0, width, axis=dim), axis, backward)
        block = jnp.concatenate([low, block, high], axis=dim)
    return block


def expert_ffn(rows, both, step=512):
    count, width = rows.shape
    hidden_units = both.shape[2]
    steps = hidden_units // step

    def body(x_ref, first_ref, second_ref, out_ref, acc_ref):
        j = pl.program_id(0)

        @pl.when(j == 0)
        def _():
            acc_ref[...] = jnp.zeros_like(acc_ref)

        h = jnp.dot(x_ref[...], first_ref[...], preferred_element_type=jnp.float32)
        h = (h / (1.0 + jnp.exp(-h))).astype(jnp.bfloat16)
        acc_ref[...] += jnp.dot(h, second_ref[...], preferred_element_type=jnp.float32)

        @pl.when(j == steps - 1)
        def _():
            out_ref[...] = acc_ref[...].astype(out_ref.dtype)

    return pl.pallas_call(
        body,
        grid=(steps,),
        in_specs=[
            pl.BlockSpec((count, width), lambda j: (0, 0)),
            pl.BlockSpec((None, width, step), lambda j: (0, 0, j)),
            pl.BlockSpec((None, step, width), lambda j: (1, j, 0)),
        ],
        out_specs=pl.BlockSpec((count, width), lambda j: (0, 0)),
        out_shape=jax.ShapeDtypeStruct((count, width), jnp.bfloat16),
        scratch_shapes=[pltpu.VMEM((count, width), jnp.float32)],
        compiler_params=pltpu.CompilerParams(dimension_semantics=("arbitrary",)),
        cost_estimate=pl.CostEstimate(
            flops=4 * count * width * hidden_units,
            transcendentals=count * hidden_units,
            bytes_accessed=2 * (2 * count * width + 2 * width * hidden_units),
        ),
    )(rows, both, both)


def layer_norm(values, gain):
    centre = jnp.mean(values, axis=-1, keepdims=True)
    centred = values - centre
    spread = jnp.mean(centred * centred, axis=-1, keepdims=True)
    return centred * lax.rsqrt(spread + eps_norm) * gain


def shards(frames, ln_gain, kernel, bn_scale, bn_shift, ffn_gain, expert_ids, gates, w_in, w_out):
    frame_count = frames.shape[1]
    width = frames.shape[2]
    taps = kernel.shape[0]
    reach = (taps - 1) // 2
    picks_per = expert_ids.shape[2]
    experts_all = lax.axis_size("expert") * w_in.shape[0]
    capacity = 2 * picks_per * frame_count // experts_all
    slots_all = experts_all * capacity
    both = lax.all_gather(jnp.concatenate([w_in, w_out], axis=0), "fsdp", axis=1, tiled=True)
    raw = padded_2(frames[0], (("expert", 0),), reach)
    padded = layer_norm(raw.astype(jnp.float32), ln_gain).astype(jnp.bfloat16)
    stream = frames[0].astype(jnp.float32)
    filtered = jnp.zeros(stream.shape, jnp.float32)
    for offset in range(taps):
        filtered = filtered + kernel[offset] * padded[offset : offset + frame_count]
    mixed = stream + jax.nn.silu(bn_scale * filtered + bn_shift)
    routed = layer_norm(mixed, ffn_gain).astype(jnp.bfloat16)
    chosen = expert_ids[0].reshape(-1)
    picks = chosen.shape[0]
    onehot = (chosen[:, None] == jnp.arange(experts_all, dtype=jnp.int32)[None, :]).astype(
        jnp.bfloat16
    )
    lower = (
        jnp.arange(picks, dtype=jnp.int32)[:, None] > jnp.arange(picks, dtype=jnp.int32)[None, :]
    ).astype(jnp.bfloat16)
    before = jnp.dot(lower, onehot, preferred_element_type=jnp.float32)
    slot_at = jnp.sum(before * onehot.astype(jnp.float32), axis=1).astype(jnp.int32)
    target = (chosen * capacity + slot_at).reshape(frame_count, picks_per)
    placing = jnp.any(
        target[None, :, :] == jnp.arange(slots_all, dtype=jnp.int32)[:, None, None], axis=2
    )
    outgoing = jnp.dot(placing.astype(jnp.bfloat16), routed, preferred_element_type=jnp.float32)
    outgoing = outgoing.astype(jnp.bfloat16).reshape(experts_all, capacity, width)
    block = lax.all_to_all(outgoing, "expert", split_axis=0, concat_axis=0, tiled=True)
    rows_in = block.reshape(-1, width)
    result = expert_ffn(rows_in, both)
    returned = lax.all_to_all(
        result.reshape(block.shape), "expert", split_axis=0, concat_axis=0, tiled=True
    )
    rows_back = returned.reshape(-1, width)
    select = (
        target.reshape(-1)[:, None] == jnp.arange(slots_all, dtype=jnp.int32)[None, :]
    ).astype(jnp.bfloat16)
    picked = jnp.dot(select, rows_back, preferred_element_type=jnp.float32).reshape(
        frame_count, picks_per, width
    )
    combined = gates[0][:, 0][:, None] * picked[:, 0]
    for k in range(1, picks_per):
        combined = combined + gates[0][:, k][:, None] * picked[:, k]
    return (mixed + 0.5 * combined).astype(jnp.bfloat16)[None]


def solution(mesh):
    return jax.shard_map(
        shards,
        mesh=mesh,
        in_specs=(
            P("fsdp", "expert", None),
            P(),
            P(),
            P(),
            P(),
            P(),
            P("fsdp", "expert", None),
            P("fsdp", "expert", None),
            P("expert", "fsdp", None),
            P("expert", "fsdp", None),
        ),
        out_specs=P("fsdp", "expert", None),
        check_vma=False,
    )
```

```python
import jax
import jax.numpy as jnp
from jax import lax
from jax.experimental import pallas as pl
from jax.experimental.pallas import tpu as pltpu
from jax.sharding import PartitionSpec as P

eps_norm = 1e-05


def padded_2(block, sides, width):
    for axis, dim in sides:
        count = lax.axis_size(axis)
        forward = [(i, i + 1) for i in range(count - 1)]
        backward = [(target, source) for source, target in forward]
        low = lax.ppermute(
            lax.slice_in_dim(block, block.shape[dim] - width, None, axis=dim), axis, forward
        )
        high = lax.ppermute(lax.slice_in_dim(block, 0, width, axis=dim), axis, backward)
        block = jnp.concatenate([low, block, high], axis=dim)
    return block


def expert_ffn(rows, both, step=768):
    count, width = rows.shape
    hidden_units = both.shape[2]
    steps = hidden_units // step

    def body(x_ref, first_ref, second_ref, out_ref, acc_ref):
        j = pl.program_id(0)

        @pl.when(j == 0)
        def _():
            acc_ref[...] = jnp.zeros_like(acc_ref)

        h = jnp.dot(x_ref[...], first_ref[...], preferred_element_type=jnp.float32)
        h = (h / (1.0 + jnp.exp(-h))).astype(jnp.bfloat16)
        acc_ref[...] += jnp.dot(h, second_ref[...], preferred_element_type=jnp.float32)

        @pl.when(j == steps - 1)
        def _():
            out_ref[...] = acc_ref[...].astype(out_ref.dtype)

    return pl.pallas_call(
        body,
        grid=(steps,),
        in_specs=[
            pl.BlockSpec((count, width), lambda j: (0, 0)),
            pl.BlockSpec((None, width, step), lambda j: (0, 0, j)),
            pl.BlockSpec((None, step, width), lambda j: (1, j, 0)),
        ],
        out_specs=pl.BlockSpec((count, width), lambda j: (0, 0)),
        out_shape=jax.ShapeDtypeStruct((count, width), jnp.bfloat16),
        scratch_shapes=[pltpu.VMEM((count, width), jnp.float32)],
        compiler_params=pltpu.CompilerParams(dimension_semantics=("arbitrary",)),
        cost_estimate=pl.CostEstimate(
            flops=4 * count * width * hidden_units,
            transcendentals=count * hidden_units,
            bytes_accessed=2 * (2 * count * width + 2 * width * hidden_units),
        ),
    )(rows, both, both)


def layer_norm(values, gain):
    centre = jnp.mean(values, axis=-1, keepdims=True)
    centred = values - centre
    spread = jnp.mean(centred * centred, axis=-1, keepdims=True)
    return centred * lax.rsqrt(spread + eps_norm) * gain


def shards(frames, ln_gain, kernel, bn_scale, bn_shift, ffn_gain, expert_ids, gates, w_in, w_out):
    frame_count = frames.shape[1]
    width = frames.shape[2]
    taps = kernel.shape[0]
    reach = (taps - 1) // 2
    picks_per = expert_ids.shape[2]
    experts_all = lax.axis_size("expert") * w_in.shape[0]
    capacity = 2 * picks_per * frame_count // experts_all
    slots_all = experts_all * capacity
    both = lax.all_gather(jnp.concatenate([w_in, w_out], axis=0), "fsdp", axis=1, tiled=True)
    raw = padded_2(frames[0], (("expert", 0),), reach)
    padded = layer_norm(raw.astype(jnp.float32), ln_gain).astype(jnp.bfloat16)
    stream = frames[0].astype(jnp.float32)
    filtered = jnp.zeros(stream.shape, jnp.float32)
    for offset in range(taps):
        filtered = filtered + kernel[offset] * padded[offset : offset + frame_count]
    mixed = stream + jax.nn.silu(bn_scale * filtered + bn_shift)
    routed = layer_norm(mixed, ffn_gain).astype(jnp.bfloat16)
    chosen = expert_ids[0].reshape(-1)
    picks = chosen.shape[0]
    onehot = (chosen[:, None] == jnp.arange(experts_all, dtype=jnp.int32)[None, :]).astype(
        jnp.bfloat16
    )
    lower = (
        jnp.arange(picks, dtype=jnp.int32)[:, None] > jnp.arange(picks, dtype=jnp.int32)[None, :]
    ).astype(jnp.bfloat16)
    before = jnp.dot(lower, onehot, preferred_element_type=jnp.float32)
    slot_at = jnp.sum(before * onehot.astype(jnp.float32), axis=1).astype(jnp.int32)
    target = (chosen * capacity + slot_at).reshape(frame_count, picks_per)
    placing = jnp.any(
        target[None, :, :] == jnp.arange(slots_all, dtype=jnp.int32)[:, None, None], axis=2
    )
    outgoing = jnp.dot(placing.astype(jnp.bfloat16), routed, preferred_element_type=jnp.float32)
    outgoing = outgoing.astype(jnp.bfloat16).reshape(experts_all, capacity, width)
    block = lax.all_to_all(outgoing, "expert", split_axis=0, concat_axis=0, tiled=True)
    rows_in = block.reshape(-1, width)
    result = expert_ffn(rows_in, both)
    returned = lax.all_to_all(
        result.reshape(block.shape), "expert", split_axis=0, concat_axis=0, tiled=True
    )
    rows_back = returned.reshape(-1, width)
    select = (
        target.reshape(-1)[:, None] == jnp.arange(slots_all, dtype=jnp.int32)[None, :]
    ).astype(jnp.bfloat16)
    picked = jnp.dot(select, rows_back, preferred_element_type=jnp.float32).reshape(
        frame_count, picks_per, width
    )
    combined = gates[0][:, 0][:, None] * picked[:, 0]
    for k in range(1, picks_per):
        combined = combined + gates[0][:, k][:, None] * picked[:, k]
    return (mixed + 0.5 * combined).astype(jnp.bfloat16)[None]


def solution(mesh):
    return jax.shard_map(
        shards,
        mesh=mesh,
        in_specs=(
            P("fsdp", "expert", None),
            P(),
            P(),
            P(),
            P(),
            P(),
            P("fsdp", "expert", None),
            P("fsdp", "expert", None),
            P("expert", "fsdp", None),
            P("expert", "fsdp", None),
        ),
        out_specs=P("fsdp", "expert", None),
        check_vma=False,
    )
```

```python
import jax
import jax.numpy as jnp
from jax import lax
from jax.experimental import pallas as pl
from jax.experimental.pallas import tpu as pltpu
from jax.sharding import PartitionSpec as P

eps_norm = 1e-05


def padded_2(block, sides, width):
    for axis, dim in sides:
        count = lax.axis_size(axis)
        forward = [(i, i + 1) for i in range(count - 1)]
        backward = [(target, source) for source, target in forward]
        low = lax.ppermute(
            lax.slice_in_dim(block, block.shape[dim] - width, None, axis=dim), axis, forward
        )
        high = lax.ppermute(lax.slice_in_dim(block, 0, width, axis=dim), axis, backward)
        block = jnp.concatenate([low, block, high], axis=dim)
    return block


def expert_ffn(rows, both, step=512):
    count, width = rows.shape
    hidden_units = both.shape[2]
    steps = hidden_units // step

    def body(x_ref, first_ref, second_ref, out_ref, acc_ref):
        j = pl.program_id(0)

        @pl.when(j == 0)
        def _():
            acc_ref[...] = jnp.zeros_like(acc_ref)

        h = jnp.dot(x_ref[...], first_ref[...], preferred_element_type=jnp.float32)
        h = (h / (1.0 + jnp.exp(-h))).astype(jnp.bfloat16)
        acc_ref[...] += jnp.dot(h, second_ref[...], preferred_element_type=jnp.float32)

        @pl.when(j == steps - 1)
        def _():
            out_ref[...] = acc_ref[...].astype(out_ref.dtype)

    return pl.pallas_call(
        body,
        grid=(steps,),
        in_specs=[
            pl.BlockSpec((count, width), lambda j: (0, 0)),
            pl.BlockSpec((None, width, step), lambda j: (0, 0, j)),
            pl.BlockSpec((None, step, width), lambda j: (1, j, 0)),
        ],
        out_specs=pl.BlockSpec((count, width), lambda j: (0, 0)),
        out_shape=jax.ShapeDtypeStruct((count, width), jnp.bfloat16),
        scratch_shapes=[pltpu.VMEM((count, width), jnp.float32)],
        compiler_params=pltpu.CompilerParams(dimension_semantics=("arbitrary",)),
        cost_estimate=pl.CostEstimate(
            flops=4 * count * width * hidden_units,
            transcendentals=count * hidden_units,
            bytes_accessed=2 * (2 * count * width + 2 * width * hidden_units),
        ),
    )(rows, both, both)


def stack_pair(first, second):
    def body(first_ref, second_ref, out_ref):
        out_ref[0] = first_ref[0]
        out_ref[1] = second_ref[0]

    return pl.pallas_call(
        body, out_shape=jax.ShapeDtypeStruct((2,) + first.shape[1:], first.dtype)
    )(first, second)


def layer_norm(values, gain):
    centre = jnp.mean(values, axis=-1, keepdims=True)
    centred = values - centre
    spread = jnp.mean(centred * centred, axis=-1, keepdims=True)
    return centred * lax.rsqrt(spread + eps_norm) * gain


def shards(frames, ln_gain, kernel, bn_scale, bn_shift, ffn_gain, expert_ids, gates, w_in, w_out):
    frame_count = frames.shape[1]
    width = frames.shape[2]
    taps = kernel.shape[0]
    reach = (taps - 1) // 2
    picks_per = expert_ids.shape[2]
    experts_all = lax.axis_size("expert") * w_in.shape[0]
    capacity = 2 * picks_per * frame_count // experts_all
    slots_all = experts_all * capacity
    both = lax.all_gather(stack_pair(w_in, w_out), "fsdp", axis=1, tiled=True)
    raw = padded_2(frames[0], (("expert", 0),), reach)
    stream = frames[0].astype(jnp.float32)
    normed = lax.optimization_barrier(layer_norm(stream, ln_gain).astype(jnp.bfloat16))
    edges = layer_norm(
        jnp.concatenate([raw[:reach], raw[reach + frame_count :]]).astype(jnp.float32), ln_gain
    ).astype(jnp.bfloat16)
    padded = jnp.concatenate([edges[:reach], normed, edges[reach:]])
    filtered = jnp.zeros(stream.shape, jnp.float32)
    for offset in range(taps):
        filtered = filtered + kernel[offset] * padded[offset : offset + frame_count]
    mixed = stream + jax.nn.silu(bn_scale * filtered + bn_shift)
    routed = layer_norm(mixed, ffn_gain).astype(jnp.bfloat16)
    chosen = expert_ids[0].reshape(-1)
    picks = chosen.shape[0]
    onehot = (chosen[:, None] == jnp.arange(experts_all, dtype=jnp.int32)[None, :]).astype(
        jnp.bfloat16
    )
    lower = (
        jnp.arange(picks, dtype=jnp.int32)[:, None] > jnp.arange(picks, dtype=jnp.int32)[None, :]
    ).astype(jnp.bfloat16)
    before = jnp.dot(lower, onehot, preferred_element_type=jnp.float32)
    slot_at = jnp.sum(before * onehot.astype(jnp.float32), axis=1).astype(jnp.int32)
    target = (chosen * capacity + slot_at).reshape(frame_count, picks_per)
    placing = jnp.any(
        target[None, :, :] == jnp.arange(slots_all, dtype=jnp.int32)[:, None, None], axis=2
    )
    outgoing = jnp.dot(placing.astype(jnp.bfloat16), routed, preferred_element_type=jnp.float32)
    outgoing = outgoing.astype(jnp.bfloat16).reshape(experts_all, capacity, width)
    block = lax.all_to_all(outgoing, "expert", split_axis=0, concat_axis=0, tiled=True)
    rows_in = block.reshape(-1, width)
    result = expert_ffn(rows_in, both)
    returned = lax.all_to_all(
        result.reshape(block.shape), "expert", split_axis=0, concat_axis=0, tiled=True
    )
    rows_back = returned.reshape(-1, width)
    select = (
        target.reshape(-1)[:, None] == jnp.arange(slots_all, dtype=jnp.int32)[None, :]
    ).astype(jnp.bfloat16)
    picked = jnp.dot(select, rows_back, preferred_element_type=jnp.float32).reshape(
        frame_count, picks_per, width
    )
    combined = gates[0][:, 0][:, None] * picked[:, 0]
    for k in range(1, picks_per):
        combined = combined + gates[0][:, k][:, None] * picked[:, k]
    return (mixed + 0.5 * combined).astype(jnp.bfloat16)[None]


def solution(mesh):
    return jax.shard_map(
        shards,
        mesh=mesh,
        in_specs=(
            P("fsdp", "expert", None),
            P(),
            P(),
            P(),
            P(),
            P(),
            P("fsdp", "expert", None),
            P("fsdp", "expert", None),
            P("expert", "fsdp", None),
            P("expert", "fsdp", None),
        ),
        out_specs=P("fsdp", "expert", None),
        check_vma=False,
    )
```

```python
import jax
import jax.numpy as jnp
from jax import lax
from jax.experimental import pallas as pl
from jax.experimental.pallas import tpu as pltpu
from jax.sharding import PartitionSpec as P

eps_norm = 1e-05


def padded_2(block, sides, width):
    for axis, dim in sides:
        count = lax.axis_size(axis)
        forward = [(i, i + 1) for i in range(count - 1)]
        backward = [(target, source) for source, target in forward]
        low = lax.ppermute(
            lax.slice_in_dim(block, block.shape[dim] - width, None, axis=dim), axis, forward
        )
        high = lax.ppermute(lax.slice_in_dim(block, 0, width, axis=dim), axis, backward)
        block = jnp.concatenate([low, block, high], axis=dim)
    return block


def expert_ffn(rows, both, step=512):
    count, width = rows.shape
    hidden_units = both.shape[2] // 2
    steps = hidden_units // step

    def body(x_ref, first_ref, second_ref, out_ref, acc_ref):
        j = pl.program_id(0)

        @pl.when(j == 0)
        def _():
            acc_ref[...] = jnp.zeros_like(acc_ref)

        h = jnp.dot(x_ref[...], first_ref[...], preferred_element_type=jnp.float32)
        h = (h / (1.0 + jnp.exp(-h))).astype(jnp.bfloat16)
        acc_ref[...] += jnp.dot(h, second_ref[...], preferred_element_type=jnp.float32)

        @pl.when(j == steps - 1)
        def _():
            out_ref[...] = acc_ref[...].astype(out_ref.dtype)

    return pl.pallas_call(
        body,
        grid=(steps,),
        in_specs=[
            pl.BlockSpec((count, width), lambda j: (0, 0)),
            pl.BlockSpec((None, width, step), lambda j: (0, 0, j)),
            pl.BlockSpec((None, step, width), lambda j: (0, j, 1)),
        ],
        out_specs=pl.BlockSpec((count, width), lambda j: (0, 0)),
        out_shape=jax.ShapeDtypeStruct((count, width), jnp.bfloat16),
        scratch_shapes=[pltpu.VMEM((count, width), jnp.float32)],
        compiler_params=pltpu.CompilerParams(dimension_semantics=("arbitrary",)),
        cost_estimate=pl.CostEstimate(
            flops=4 * count * width * hidden_units,
            transcendentals=count * hidden_units,
            bytes_accessed=2 * (2 * count * width + 2 * width * hidden_units),
        ),
    )(rows, both, both)


def layer_norm(values, gain):
    centre = jnp.mean(values, axis=-1, keepdims=True)
    centred = values - centre
    spread = jnp.mean(centred * centred, axis=-1, keepdims=True)
    return centred * lax.rsqrt(spread + eps_norm) * gain


def shards(frames, ln_gain, kernel, bn_scale, bn_shift, ffn_gain, expert_ids, gates, w_in, w_out):
    frame_count = frames.shape[1]
    width = frames.shape[2]
    taps = kernel.shape[0]
    reach = (taps - 1) // 2
    picks_per = expert_ids.shape[2]
    experts_all = lax.axis_size("expert") * w_in.shape[0]
    capacity = 2 * picks_per * frame_count // experts_all
    slots_all = experts_all * capacity
    both = lax.all_gather(jnp.concatenate([w_in, w_out], axis=2), "fsdp", axis=1, tiled=True)
    raw = padded_2(frames[0], (("expert", 0),), reach)
    padded = layer_norm(raw.astype(jnp.float32), ln_gain).astype(jnp.bfloat16)
    stream = frames[0].astype(jnp.float32)
    filtered = jnp.zeros(stream.shape, jnp.float32)
    for offset in range(taps):
        filtered = filtered + kernel[offset] * padded[offset : offset + frame_count]
    mixed = stream + jax.nn.silu(bn_scale * filtered + bn_shift)
    routed = layer_norm(mixed, ffn_gain).astype(jnp.bfloat16)
    chosen = expert_ids[0].reshape(-1)
    picks = chosen.shape[0]
    onehot = (chosen[:, None] == jnp.arange(experts_all, dtype=jnp.int32)[None, :]).astype(
        jnp.bfloat16
    )
    lower = (
        jnp.arange(picks, dtype=jnp.int32)[:, None] > jnp.arange(picks, dtype=jnp.int32)[None, :]
    ).astype(jnp.bfloat16)
    before = jnp.dot(lower, onehot, preferred_element_type=jnp.float32)
    slot_at = jnp.sum(before * onehot.astype(jnp.float32), axis=1).astype(jnp.int32)
    target = (chosen * capacity + slot_at).reshape(frame_count, picks_per)
    placing = jnp.any(
        target[None, :, :] == jnp.arange(slots_all, dtype=jnp.int32)[:, None, None], axis=2
    )
    outgoing = jnp.dot(placing.astype(jnp.bfloat16), routed, preferred_element_type=jnp.float32)
    outgoing = outgoing.astype(jnp.bfloat16).reshape(experts_all, capacity, width)
    block = lax.all_to_all(outgoing, "expert", split_axis=0, concat_axis=0, tiled=True)
    rows_in = block.reshape(-1, width)
    result = expert_ffn(rows_in, both)
    returned = lax.all_to_all(
        result.reshape(block.shape), "expert", split_axis=0, concat_axis=0, tiled=True
    )
    rows_back = returned.reshape(-1, width)
    select = (
        target.reshape(-1)[:, None] == jnp.arange(slots_all, dtype=jnp.int32)[None, :]
    ).astype(jnp.bfloat16)
    picked = jnp.dot(select, rows_back, preferred_element_type=jnp.float32).reshape(
        frame_count, picks_per, width
    )
    combined = gates[0][:, 0][:, None] * picked[:, 0]
    for k in range(1, picks_per):
        combined = combined + gates[0][:, k][:, None] * picked[:, k]
    return (mixed + 0.5 * combined).astype(jnp.bfloat16)[None]


def solution(mesh):
    return jax.shard_map(
        shards,
        mesh=mesh,
        in_specs=(
            P("fsdp", "expert", None),
            P(),
            P(),
            P(),
            P(),
            P(),
            P("fsdp", "expert", None),
            P("fsdp", "expert", None),
            P("expert", "fsdp", None),
            P("expert", "fsdp", None),
        ),
        out_specs=P("fsdp", "expert", None),
        check_vma=False,
    )
```

```python
import jax
import jax.numpy as jnp
from jax import lax
from jax.experimental import pallas as pl
from jax.experimental.pallas import tpu as pltpu
from jax.sharding import PartitionSpec as P

eps_norm = 1e-05


def padded_2(block, sides, width):
    for axis, dim in sides:
        count = lax.axis_size(axis)
        forward = [(i, i + 1) for i in range(count - 1)]
        backward = [(target, source) for source, target in forward]
        low = lax.ppermute(
            lax.slice_in_dim(block, block.shape[dim] - width, None, axis=dim), axis, forward
        )
        high = lax.ppermute(lax.slice_in_dim(block, 0, width, axis=dim), axis, backward)
        block = jnp.concatenate([low, block, high], axis=dim)
    return block


def expert_ffn(rows, both, step=512):
    count, width = rows.shape
    hidden_units = both.shape[2] // 2
    steps = hidden_units // step

    def body(x_ref, first_ref, second_ref, out_ref, acc_ref):
        j = pl.program_id(0)

        @pl.when(j == 0)
        def _():
            acc_ref[...] = jnp.zeros_like(acc_ref)

        h = jnp.dot(x_ref[...], first_ref[...], preferred_element_type=jnp.float32)
        h = (h / (1.0 + jnp.exp(-h))).astype(jnp.bfloat16)
        acc_ref[...] += jnp.dot(h, second_ref[...], preferred_element_type=jnp.float32)

        @pl.when(j == steps - 1)
        def _():
            out_ref[...] = acc_ref[...].astype(out_ref.dtype)

    return pl.pallas_call(
        body,
        grid=(steps,),
        in_specs=[
            pl.BlockSpec((count, width), lambda j: (0, 0)),
            pl.BlockSpec((None, width, step), lambda j: (0, 0, j)),
            pl.BlockSpec((None, step, width), lambda j: (0, j, 1)),
        ],
        out_specs=pl.BlockSpec((count, width), lambda j: (0, 0)),
        out_shape=jax.ShapeDtypeStruct((count, width), jnp.bfloat16),
        scratch_shapes=[pltpu.VMEM((count, width), jnp.float32)],
        compiler_params=pltpu.CompilerParams(dimension_semantics=("arbitrary",)),
        cost_estimate=pl.CostEstimate(
            flops=4 * count * width * hidden_units,
            transcendentals=count * hidden_units,
            bytes_accessed=2 * (2 * count * width + 2 * width * hidden_units),
        ),
    )(rows, both, both)


def layer_norm(values, gain):
    centre = jnp.mean(values, axis=-1, keepdims=True)
    centred = values - centre
    spread = jnp.mean(centred * centred, axis=-1, keepdims=True)
    return centred * lax.rsqrt(spread + eps_norm) * gain


def shards(frames, ln_gain, kernel, bn_scale, bn_shift, ffn_gain, expert_ids, gates, w_in, w_out):
    frame_count = frames.shape[1]
    width = frames.shape[2]
    taps = kernel.shape[0]
    reach = (taps - 1) // 2
    picks_per = expert_ids.shape[2]
    experts_all = lax.axis_size("expert") * w_in.shape[0]
    capacity = 2 * picks_per * frame_count // experts_all
    slots_all = experts_all * capacity
    both = lax.all_gather(jnp.concatenate([w_in, w_out], axis=2), "fsdp", axis=1, tiled=True)
    raw = padded_2(frames[0], (("expert", 0),), reach)
    stream = frames[0].astype(jnp.float32)
    normed = layer_norm(stream, ln_gain).astype(jnp.bfloat16)
    edges = layer_norm(
        jnp.concatenate([raw[:reach], raw[reach + frame_count :]]).astype(jnp.float32), ln_gain
    ).astype(jnp.bfloat16)
    padded = jnp.concatenate([edges[:reach], normed, edges[reach:]])
    filtered = jnp.zeros(stream.shape, jnp.float32)
    for offset in range(taps):
        filtered = filtered + kernel[offset] * padded[offset : offset + frame_count]
    mixed = stream + jax.nn.silu(bn_scale * filtered + bn_shift)
    routed = layer_norm(mixed, ffn_gain).astype(jnp.bfloat16)
    chosen = expert_ids[0].reshape(-1)
    picks = chosen.shape[0]
    onehot = (chosen[:, None] == jnp.arange(experts_all, dtype=jnp.int32)[None, :]).astype(
        jnp.bfloat16
    )
    lower = (
        jnp.arange(picks, dtype=jnp.int32)[:, None] > jnp.arange(picks, dtype=jnp.int32)[None, :]
    ).astype(jnp.bfloat16)
    before = jnp.dot(lower, onehot, preferred_element_type=jnp.float32)
    slot_at = jnp.sum(before * onehot.astype(jnp.float32), axis=1).astype(jnp.int32)
    target = (chosen * capacity + slot_at).reshape(frame_count, picks_per)
    placing = jnp.any(
        target[None, :, :] == jnp.arange(slots_all, dtype=jnp.int32)[:, None, None], axis=2
    )
    outgoing = jnp.dot(placing.astype(jnp.bfloat16), routed, preferred_element_type=jnp.float32)
    outgoing = outgoing.astype(jnp.bfloat16).reshape(experts_all, capacity, width)
    block = lax.all_to_all(outgoing, "expert", split_axis=0, concat_axis=0, tiled=True)
    rows_in = block.reshape(-1, width)
    result = expert_ffn(rows_in, both)
    returned = lax.all_to_all(
        result.reshape(block.shape), "expert", split_axis=0, concat_axis=0, tiled=True
    )
    rows_back = returned.reshape(-1, width)
    select = (
        target.reshape(-1)[:, None] == jnp.arange(slots_all, dtype=jnp.int32)[None, :]
    ).astype(jnp.bfloat16)
    picked = jnp.dot(select, rows_back, preferred_element_type=jnp.float32).reshape(
        frame_count, picks_per, width
    )
    combined = gates[0][:, 0][:, None] * picked[:, 0]
    for k in range(1, picks_per):
        combined = combined + gates[0][:, k][:, None] * picked[:, k]
    return (mixed + 0.5 * combined).astype(jnp.bfloat16)[None]


def solution(mesh):
    return jax.shard_map(
        shards,
        mesh=mesh,
        in_specs=(
            P("fsdp", "expert", None),
            P(),
            P(),
            P(),
            P(),
            P(),
            P("fsdp", "expert", None),
            P("fsdp", "expert", None),
            P("expert", "fsdp", None),
            P("expert", "fsdp", None),
        ),
        out_specs=P("fsdp", "expert", None),
        check_vma=False,
    )
```

```python
import jax
import jax.numpy as jnp
from jax import lax
from jax.experimental import pallas as pl
from jax.experimental.pallas import tpu as pltpu
from jax.sharding import PartitionSpec as P

eps_norm = 1e-05


def padded_2(block, sides, width):
    for axis, dim in sides:
        count = lax.axis_size(axis)
        forward = [(i, i + 1) for i in range(count - 1)]
        backward = [(target, source) for source, target in forward]
        low = lax.ppermute(
            lax.slice_in_dim(block, block.shape[dim] - width, None, axis=dim), axis, forward
        )
        high = lax.ppermute(lax.slice_in_dim(block, 0, width, axis=dim), axis, backward)
        block = jnp.concatenate([low, block, high], axis=dim)
    return block


def expert_ffn(rows, both, step=512, tiles=2):
    count, width = rows.shape
    hidden_units = both.shape[2] // 2
    steps = hidden_units // step
    tile = count // tiles

    def body(x_ref, first_ref, second_ref, out_ref, acc_ref):
        j = pl.program_id(1)

        @pl.when(j == 0)
        def _():
            acc_ref[...] = jnp.zeros_like(acc_ref)

        h = jnp.dot(x_ref[...], first_ref[...], preferred_element_type=jnp.float32)
        h = (h / (1.0 + jnp.exp(-h))).astype(jnp.bfloat16)
        acc_ref[...] += jnp.dot(h, second_ref[...], preferred_element_type=jnp.float32)

        @pl.when(j == steps - 1)
        def _():
            out_ref[...] = acc_ref[...].astype(out_ref.dtype)

    return pl.pallas_call(
        body,
        grid=(tiles, steps),
        in_specs=[
            pl.BlockSpec((tile, width), lambda m, j: (m, 0)),
            pl.BlockSpec((None, width, step), lambda m, j: (0, 0, j)),
            pl.BlockSpec((None, step, width), lambda m, j: (0, j, 1)),
        ],
        out_specs=pl.BlockSpec((tile, width), lambda m, j: (m, 0)),
        out_shape=jax.ShapeDtypeStruct((count, width), jnp.bfloat16),
        scratch_shapes=[pltpu.VMEM((tile, width), jnp.float32)],
        compiler_params=pltpu.CompilerParams(dimension_semantics=("arbitrary", "arbitrary")),
        cost_estimate=pl.CostEstimate(
            flops=4 * count * width * hidden_units,
            transcendentals=count * hidden_units,
            bytes_accessed=2 * (2 * count * width + 2 * tiles * width * hidden_units),
        ),
    )(rows, both, both)


def layer_norm(values, gain):
    centre = jnp.mean(values, axis=-1, keepdims=True)
    centred = values - centre
    spread = jnp.mean(centred * centred, axis=-1, keepdims=True)
    return centred * lax.rsqrt(spread + eps_norm) * gain


def shards(frames, ln_gain, kernel, bn_scale, bn_shift, ffn_gain, expert_ids, gates, w_in, w_out):
    frame_count = frames.shape[1]
    width = frames.shape[2]
    taps = kernel.shape[0]
    reach = (taps - 1) // 2
    picks_per = expert_ids.shape[2]
    experts_all = lax.axis_size("expert") * w_in.shape[0]
    capacity = 2 * picks_per * frame_count // experts_all
    slots_all = experts_all * capacity
    both = lax.all_gather(jnp.concatenate([w_in, w_out], axis=2), "fsdp", axis=1, tiled=True)
    raw = padded_2(frames[0], (("expert", 0),), reach)
    stream = frames[0].astype(jnp.float32)
    normed = layer_norm(stream, ln_gain).astype(jnp.bfloat16)
    edges = layer_norm(
        jnp.concatenate([raw[:reach], raw[reach + frame_count :]]).astype(jnp.float32), ln_gain
    ).astype(jnp.bfloat16)
    padded = jnp.concatenate([edges[:reach], normed, edges[reach:]])
    filtered = jnp.zeros(stream.shape, jnp.float32)
    for offset in range(taps):
        filtered = filtered + kernel[offset] * padded[offset : offset + frame_count]
    mixed = stream + jax.nn.silu(bn_scale * filtered + bn_shift)
    routed = layer_norm(mixed, ffn_gain).astype(jnp.bfloat16)
    chosen = expert_ids[0].reshape(-1)
    picks = chosen.shape[0]
    onehot = (chosen[:, None] == jnp.arange(experts_all, dtype=jnp.int32)[None, :]).astype(
        jnp.bfloat16
    )
    lower = (
        jnp.arange(picks, dtype=jnp.int32)[:, None] > jnp.arange(picks, dtype=jnp.int32)[None, :]
    ).astype(jnp.bfloat16)
    before = jnp.dot(lower, onehot, preferred_element_type=jnp.float32)
    slot_at = jnp.sum(before * onehot.astype(jnp.float32), axis=1).astype(jnp.int32)
    target = (chosen * capacity + slot_at).reshape(frame_count, picks_per)
    placing = jnp.any(
        target[None, :, :] == jnp.arange(slots_all, dtype=jnp.int32)[:, None, None], axis=2
    )
    outgoing = jnp.dot(placing.astype(jnp.bfloat16), routed, preferred_element_type=jnp.float32)
    outgoing = outgoing.astype(jnp.bfloat16).reshape(experts_all, capacity, width)
    block = lax.all_to_all(outgoing, "expert", split_axis=0, concat_axis=0, tiled=True)
    rows_in = block.reshape(-1, width)
    result = expert_ffn(rows_in, both)
    returned = lax.all_to_all(
        result.reshape(block.shape), "expert", split_axis=0, concat_axis=0, tiled=True
    )
    rows_back = returned.reshape(-1, width)
    select = (
        target.reshape(-1)[:, None] == jnp.arange(slots_all, dtype=jnp.int32)[None, :]
    ).astype(jnp.bfloat16)
    picked = jnp.dot(select, rows_back, preferred_element_type=jnp.float32).reshape(
        frame_count, picks_per, width
    )
    combined = gates[0][:, 0][:, None] * picked[:, 0]
    for k in range(1, picks_per):
        combined = combined + gates[0][:, k][:, None] * picked[:, k]
    return (mixed + 0.5 * combined).astype(jnp.bfloat16)[None]


def solution(mesh):
    return jax.shard_map(
        shards,
        mesh=mesh,
        in_specs=(
            P("fsdp", "expert", None),
            P(),
            P(),
            P(),
            P(),
            P(),
            P("fsdp", "expert", None),
            P("fsdp", "expert", None),
            P("expert", "fsdp", None),
            P("expert", "fsdp", None),
        ),
        out_specs=P("fsdp", "expert", None),
        check_vma=False,
    )
```

```python
import jax
import jax.numpy as jnp
from jax import lax
from jax.experimental import pallas as pl
from jax.experimental.pallas import tpu as pltpu
from jax.sharding import PartitionSpec as P

eps_norm = 1e-05


def padded_2(block, sides, width):
    for axis, dim in sides:
        count = lax.axis_size(axis)
        forward = [(i, i + 1) for i in range(count - 1)]
        backward = [(target, source) for source, target in forward]
        low = lax.ppermute(
            lax.slice_in_dim(block, block.shape[dim] - width, None, axis=dim), axis, forward
        )
        high = lax.ppermute(lax.slice_in_dim(block, 0, width, axis=dim), axis, backward)
        block = jnp.concatenate([low, block, high], axis=dim)
    return block


def expert_ffn(rows, both, step=512):
    count, width = rows.shape
    hidden_units = both.shape[2] // 2
    steps = hidden_units // step

    def body(x_ref, first_ref, second_ref, out_ref, acc_ref):
        j = pl.program_id(0)

        h = jnp.dot(x_ref[...], first_ref[...], preferred_element_type=jnp.float32)
        h = (h / (1.0 + jnp.exp(-h))).astype(jnp.bfloat16)
        part = jnp.dot(h, second_ref[...], preferred_element_type=jnp.float32)

        @pl.when(j == 0)
        def _():
            acc_ref[...] = part

        @pl.when(j > 0)
        def _():
            acc_ref[...] += part

        @pl.when(j == steps - 1)
        def _():
            out_ref[...] = acc_ref[...].astype(out_ref.dtype)

    return pl.pallas_call(
        body,
        grid=(steps,),
        in_specs=[
            pl.BlockSpec((count, width), lambda j: (0, 0)),
            pl.BlockSpec((None, width, step), lambda j: (0, 0, j)),
            pl.BlockSpec((None, step, width), lambda j: (0, j, 1)),
        ],
        out_specs=pl.BlockSpec((count, width), lambda j: (0, 0)),
        out_shape=jax.ShapeDtypeStruct((count, width), jnp.bfloat16),
        scratch_shapes=[pltpu.VMEM((count, width), jnp.float32)],
        compiler_params=pltpu.CompilerParams(dimension_semantics=("arbitrary",)),
        cost_estimate=pl.CostEstimate(
            flops=4 * count * width * hidden_units,
            transcendentals=count * hidden_units,
            bytes_accessed=2 * (2 * count * width + 2 * width * hidden_units),
        ),
    )(rows, both, both)


def layer_norm(values, gain):
    centre = jnp.mean(values, axis=-1, keepdims=True)
    centred = values - centre
    spread = jnp.mean(centred * centred, axis=-1, keepdims=True)
    return centred * lax.rsqrt(spread + eps_norm) * gain


def shards(frames, ln_gain, kernel, bn_scale, bn_shift, ffn_gain, expert_ids, gates, w_in, w_out):
    frame_count = frames.shape[1]
    width = frames.shape[2]
    taps = kernel.shape[0]
    reach = (taps - 1) // 2
    picks_per = expert_ids.shape[2]
    experts_all = lax.axis_size("expert") * w_in.shape[0]
    capacity = 2 * picks_per * frame_count // experts_all
    slots_all = experts_all * capacity
    both = lax.all_gather(jnp.concatenate([w_in, w_out], axis=2), "fsdp", axis=1, tiled=True)
    raw = padded_2(frames[0], (("expert", 0),), reach)
    stream = frames[0].astype(jnp.float32)
    normed = layer_norm(stream, ln_gain).astype(jnp.bfloat16)
    edges = layer_norm(
        jnp.concatenate([raw[:reach], raw[reach + frame_count :]]).astype(jnp.float32), ln_gain
    ).astype(jnp.bfloat16)
    padded = jnp.concatenate([edges[:reach], normed, edges[reach:]])
    filtered = jnp.zeros(stream.shape, jnp.float32)
    for offset in range(taps):
        filtered = filtered + kernel[offset] * padded[offset : offset + frame_count]
    mixed = stream + jax.nn.silu(bn_scale * filtered + bn_shift)
    routed = layer_norm(mixed, ffn_gain).astype(jnp.bfloat16)
    chosen = expert_ids[0].reshape(-1)
    picks = chosen.shape[0]
    onehot = (chosen[:, None] == jnp.arange(experts_all, dtype=jnp.int32)[None, :]).astype(
        jnp.bfloat16
    )
    lower = (
        jnp.arange(picks, dtype=jnp.int32)[:, None] > jnp.arange(picks, dtype=jnp.int32)[None, :]
    ).astype(jnp.bfloat16)
    before = jnp.dot(lower, onehot, preferred_element_type=jnp.float32)
    slot_at = jnp.sum(before * onehot.astype(jnp.float32), axis=1).astype(jnp.int32)
    target = (chosen * capacity + slot_at).reshape(frame_count, picks_per)
    placing = jnp.any(
        target[None, :, :] == jnp.arange(slots_all, dtype=jnp.int32)[:, None, None], axis=2
    )
    outgoing = jnp.dot(placing.astype(jnp.bfloat16), routed, preferred_element_type=jnp.float32)
    outgoing = outgoing.astype(jnp.bfloat16).reshape(experts_all, capacity, width)
    block = lax.all_to_all(outgoing, "expert", split_axis=0, concat_axis=0, tiled=True)
    rows_in = block.reshape(-1, width)
    result = expert_ffn(rows_in, both)
    returned = lax.all_to_all(
        result.reshape(block.shape), "expert", split_axis=0, concat_axis=0, tiled=True
    )
    rows_back = returned.reshape(-1, width)
    select = (
        target.reshape(-1)[:, None] == jnp.arange(slots_all, dtype=jnp.int32)[None, :]
    ).astype(jnp.bfloat16)
    picked = jnp.dot(select, rows_back, preferred_element_type=jnp.float32).reshape(
        frame_count, picks_per, width
    )
    combined = gates[0][:, 0][:, None] * picked[:, 0]
    for k in range(1, picks_per):
        combined = combined + gates[0][:, k][:, None] * picked[:, k]
    return (mixed + 0.5 * combined).astype(jnp.bfloat16)[None]


def solution(mesh):
    return jax.shard_map(
        shards,
        mesh=mesh,
        in_specs=(
            P("fsdp", "expert", None),
            P(),
            P(),
            P(),
            P(),
            P(),
            P("fsdp", "expert", None),
            P("fsdp", "expert", None),
            P("expert", "fsdp", None),
            P("expert", "fsdp", None),
        ),
        out_specs=P("fsdp", "expert", None),
        check_vma=False,
    )
```
